512 devices in a mesh: wide: 32 (over z, x), narrow: 16 (over y, core).
Axes of the slice: x: 4, y: 8, z: 8, core: 2. Of those that a mesh axis runs over, the one named last changes fastest.
Arguments:
- tokens: bfloat16 [1024, 16384], P('wide', 'narrow'), may hold values from -200 to 200
- norm_gain: float32 [16384], P('narrow'), may hold values from 0.25 to 1.75
- gate_weight: bfloat16 [26624, 16384], P('wide', 'narrow'), may hold values from -0.046875 to 0.046875
- up_weight: bfloat16 [26624, 16384], P('wide', 'narrow'), may hold values from -0.046875 to 0.046875
- down_weight: bfloat16 [26624, 16384], P('wide', 'narrow'), may hold values from -0.0390625 to 0.0390625
Outputs:
- ffn_out: bfloat16 [1024, 16384], P('wide', 'narrow')
The draws below stay inside these ranges and needn't reach their ends.
All inputs are finite; a program needn't handle non-finite values.
Results may differ from the reference program's by a relative error of at most 0.03.
Values may be sent and summed in bfloat16 or wider, within the bound.
No kernel may reach another device: no remote copies, remote signals or barrier semaphores. Data moves between devices by JAX's collectives and lax.ppermute only.
A program may use at most 64 MiB of HBM per device.

```python
import math
import jax
import jax.numpy as jnp
from jax import lax

D = 16384
FF = 26624
TOKENS = 1024
N_WIDE = 32
N_NARROW = 16


def draw_tokens(key, part):
    keys = jax.random.split(key, 3)
    ramp = jnp.exp(math.log(3.0) * jnp.arange(D, dtype=jnp.float32) / max(D - 1, 1))
    base = jnp.clip(jax.random.normal(keys[0], (TOKENS, D), jnp.float32), -4.0, 4.0)
    row_scale = 0.5 * jnp.exp(jax.random.uniform(keys[1], (TOKENS, 1), jnp.float32, 0.0, math.log(10.0)))
    col_scale = 0.3 * ramp * jnp.exp(jax.random.uniform(keys[2], (1, D), jnp.float32, 0.0, math.log(10.0)))
    return (base * row_scale * col_scale).astype(jnp.bfloat16)


def levels(key, extent, shards, least, high):
    def one(dim, blocks):
        draws = jax.random.uniform(jax.random.fold_in(jax.random.fold_in(key, 6), dim), (blocks,), jnp.float32, least / len(shards), high / len(shards))
        return jnp.repeat(jnp.exp(draws), extent[dim] // blocks).reshape((-1,) + (1,) * (len(extent) - dim - 1))

    level = one(*shards[0])
    for cut in shards[1:]:
        level = level * one(*cut)
    return level


def centred(rng, shape, width, bound, shards=(), kind=jnp.bfloat16):
    array = jax.random.normal(rng, shape, jnp.float32) * width
    if len(shards) > 0:
        array = levels(rng, shape, shards, -0.22, 0.18) * array
    return jnp.clip(array, min=-bound, max=bound).astype(kind)


def setup_inputs(seed: int = 0) -> dict:
    key_list = jax.random.split(jax.random.key(seed), 6)
    tokens = draw_tokens(jax.random.fold_in(key_list[5], 71), 0)
    norm_gain = jnp.clip(1.0 + 0.15 * jax.random.normal(key_list[1], (D,), jnp.float32), 0.25, 1.75)
    gate_weight = centred(key_list[2], (FF, D), D ** -0.5, 0.046875, ((0, 32), (1, 16)))
    up_weight = centred(key_list[3], (FF, D), D ** -0.5, 0.046875, ((0, 32), (1, 16)))
    down_weight = centred(key_list[4], (FF, D), FF ** -0.5, 0.0390625, ((0, 32), (1, 16)))
    return {"tokens": tokens, "norm_gain": norm_gain, "gate_weight": gate_weight, "up_weight": up_weight, "down_weight": down_weight}


EPS = 1e-05

def reference(tokens, norm_gain, gate_weight, up_weight, down_weight):
    values = tokens.astype(jnp.float32)
    squares = lax.optimization_barrier(jnp.sum(values * values, axis=1, keepdims=True))
    normed = (values * lax.rsqrt(squares / D + EPS) * norm_gain).astype(jnp.bfloat16)
    block = D // N_NARROW
    dims = (((1,), (1,)), ((), ()))

    def feature_block(carry, index):
        start = (index * block).astype(jnp.int32)
        rows = lax.dynamic_slice_in_dim(normed, start, block, 1)
        gate_cols = lax.dynamic_slice_in_dim(gate_weight, start, block, 1)
        up_cols = lax.dynamic_slice_in_dim(up_weight, start, block, 1)
        gate_part = lax.dot_general(rows, gate_cols, dims, preferred_element_type=jnp.float32)
        up_part = lax.dot_general(rows, up_cols, dims, preferred_element_type=jnp.float32)
        gate_part = lax.optimization_barrier(gate_part.astype(jnp.bfloat16)).astype(jnp.float32)
        up_part = lax.optimization_barrier(up_part.astype(jnp.bfloat16)).astype(jnp.float32)
        return ((carry[0] + gate_part, carry[1] + up_part), None)
    zero = jnp.zeros((TOKENS, FF), jnp.float32)
    (gate, upward), _ = lax.scan(feature_block, (zero, zero), jnp.arange(N_NARROW, dtype=jnp.int32))
    hidden = (jax.nn.silu(gate) * upward).astype(jnp.bfloat16)
    unit = FF // N_WIDE

    def hidden_block(carry, index):
        start = (index * unit).astype(jnp.int32)
        rows = lax.dynamic_slice_in_dim(hidden, start, unit, 1)
        weights = lax.dynamic_slice_in_dim(down_weight, start, unit, 0)
        part = jnp.dot(rows, weights, preferred_element_type=jnp.float32)
        part = lax.optimization_barrier(part.astype(jnp.bfloat16)).astype(jnp.float32)
        return (carry + part, None)
    total, _ = lax.scan(hidden_block, jnp.zeros((TOKENS, D), jnp.float32), jnp.arange(N_WIDE, dtype=jnp.int32))
    return total.astype(jnp.bfloat16)
```

```python
import jax
import jax.numpy as jnp
from jax import lax
from jax.sharding import PartitionSpec as P

D = 16384
EPS = 1e-05

WIDE_AG = 'a2a'
NARROW = 'rs_ag'
WIDE_RS = 'a2a'


def local(tokens, norm_gain, gate_weight, up_weight, down_weight):
    width = gate_weight.shape[0]
    n_wide = lax.axis_size("wide")
    n_narrow = lax.axis_size("narrow")
    rows = tokens.shape[0]
    if WIDE_AG == "a2a":
        spread = jnp.broadcast_to(tokens[None], (n_wide,) + tokens.shape)
        whole = lax.all_to_all(spread, "wide", 0, 0).reshape(n_wide * rows, tokens.shape[1])
    else:
        whole = lax.all_gather(tokens, "wide", axis=0, tiled=True)
    values = whole.astype(jnp.float32)
    squares = lax.psum(jnp.sum(values * values, axis=1), "narrow")
    normed = (values * lax.rsqrt(squares[:, None] / D + EPS) * norm_gain).astype(jnp.bfloat16)
    dims = (((1,), (1,)), ((), ()))
    gate = lax.dot_general(normed, gate_weight, dims, preferred_element_type=jnp.float32)
    upward = lax.dot_general(normed, up_weight, dims, preferred_element_type=jnp.float32)
    pair = jnp.concatenate([gate, upward], axis=1).astype(jnp.bfloat16)
    total = whole.shape[0]
    if NARROW == "ar":
        sums = lax.psum(pair, "narrow").astype(jnp.float32)
        hidden = (jax.nn.silu(sums[:, :width]) * sums[:, width:]).astype(jnp.bfloat16)
    else:
        if NARROW == "rs_ag":
            part = lax.psum_scatter(pair, "narrow", scatter_dimension=0, tiled=True).astype(jnp.float32)
        else:
            pieces = pair.reshape(n_narrow, total // n_narrow, 2 * width)
            part = jnp.sum(lax.all_to_all(pieces, "narrow", 0, 0).astype(jnp.float32), axis=0)
        mine = (jax.nn.silu(part[:, :width]) * part[:, width:]).astype(jnp.bfloat16)
        hidden = lax.all_gather(mine, "narrow", axis=0, tiled=True)
    down = jnp.dot(hidden, down_weight, preferred_element_type=jnp.float32).astype(jnp.bfloat16)
    if WIDE_RS == "a2a":
        pieces = down.reshape(n_wide, total // n_wide, down.shape[1])
        return jnp.sum(lax.all_to_all(pieces, "wide", 0, 0).astype(jnp.float32), axis=0).astype(jnp.bfloat16)
    return lax.psum_scatter(down, "wide", scatter_dimension=0, tiled=True)


def solution(mesh):
    in_specs = (
        P("wide", "narrow"),
        P("narrow"),
        P("wide", "narrow"),
        P("wide", "narrow"),
        P("wide", "narrow"),
    )
    out_specs = P("wide", "narrow")
    return jax.shard_map(local, mesh=mesh, in_specs=in_specs, out_specs=out_specs, check_vma=False)
```

```python
import jax
import jax.numpy as jnp
from jax import lax
from jax.sharding import PartitionSpec as P

EPS = 1e-05


def local(tokens, norm_gain, gate_weight, up_weight, down_weight):
    width = gate_weight.shape[0]
    n_wide = lax.axis_size("wide")
    n_narrow = lax.axis_size("narrow")
    model_width = tokens.shape[1] * n_narrow
    rows = tokens.shape[0]
    spread = jnp.broadcast_to(tokens[None], (n_wide,) + tokens.shape)
    whole = lax.all_to_all(spread, "wide", 0, 0).reshape(n_wide * rows, tokens.shape[1])
    values = whole.astype(jnp.float32)
    partial = jnp.sum(values * values, axis=1)
    scaled = (values * norm_gain).astype(jnp.bfloat16)
    dims = (((1,), (1,)), ((), ()))
    gate = lax.dot_general(scaled, gate_weight, dims, preferred_element_type=jnp.float32)
    upward = lax.dot_general(scaled, up_weight, dims, preferred_element_type=jnp.float32)
    pair = jnp.concatenate([gate, upward], axis=1).astype(jnp.bfloat16)
    pair, partial = lax.optimization_barrier((pair, partial))
    part = lax.psum_scatter(pair, "narrow", scatter_dimension=0, tiled=True)
    squares = lax.psum(partial, "narrow")
    step = part.shape[0]
    start = lax.axis_index("narrow") * step
    mine_sq = lax.dynamic_slice_in_dim(squares, start, step, 0)
    scale = lax.rsqrt(mine_sq / model_width + EPS)[:, None]
    sums = part.astype(jnp.float32)
    mine = (jax.nn.silu(sums[:, :width] * scale) * (sums[:, width:] * scale)).astype(jnp.bfloat16)
    hidden = lax.all_gather(mine, "narrow", axis=0, tiled=True)
    down = jnp.dot(hidden, down_weight, preferred_element_type=jnp.float32).astype(jnp.bfloat16)
    pieces = down.reshape(n_wide, down.shape[0] // n_wide, down.shape[1])
    return jnp.sum(lax.all_to_all(pieces, "wide", 0, 0).astype(jnp.float32), axis=0).astype(jnp.bfloat16)


def solution(mesh):
    in_specs = (
        P("wide", "narrow"),
        P("narrow"),
        P("wide", "narrow"),
        P("wide", "narrow"),
        P("wide", "narrow"),
    )
    out_specs = P("wide", "narrow")
    return jax.shard_map(local, mesh=mesh, in_specs=in_specs, out_specs=out_specs, check_vma=False)
```

```python
import jax
import jax.numpy as jnp
from jax import lax
from jax.sharding import Mesh, PartitionSpec as P

EPS = 1e-05
NARROW = ("y", "core")


def local(tokens, norm_gain, gate_weight, up_weight, down_weight):
    width = gate_weight.shape[0]
    n_z = lax.axis_size("z")
    n_x = lax.axis_size("x")
    n_narrow = lax.axis_size(NARROW)
    model_width = tokens.shape[1] * n_narrow
    rows = tokens.shape[0]
    spread = jnp.broadcast_to(tokens[None], (n_z,) + tokens.shape)
    near = lax.all_to_all(spread, "z", 0, 0)
    spread = jnp.broadcast_to(near[:, None], (n_z, n_x) + tokens.shape)
    whole = lax.all_to_all(spread, "x", 1, 1).reshape(n_z * n_x * rows, tokens.shape[1])
    values = whole.astype(jnp.float32)
    partial = jnp.sum(values * values, axis=1)
    scaled = (values * norm_gain).astype(jnp.bfloat16)
    dims = (((1,), (1,)), ((), ()))
    gate = lax.dot_general(scaled, gate_weight, dims, preferred_element_type=jnp.float32)
    upward = lax.dot_general(scaled, up_weight, dims, preferred_element_type=jnp.float32)
    pair = jnp.concatenate([gate, upward], axis=1).astype(jnp.bfloat16)
    pair, partial = lax.optimization_barrier((pair, partial))
    part = lax.psum_scatter(pair, NARROW, scatter_dimension=0, tiled=True)
    squares = lax.psum(partial, NARROW)
    step = part.shape[0]
    start = lax.axis_index(NARROW) * step
    mine_sq = lax.dynamic_slice_in_dim(squares, start, step, 0)
    scale = lax.rsqrt(mine_sq / model_width + EPS)[:, None]
    sums = part.astype(jnp.float32)
    mine = (jax.nn.silu(sums[:, :width] * scale) * (sums[:, width:] * scale)).astype(jnp.bfloat16)
    half = width // 2
    first = lax.all_gather(mine[:, :half], NARROW, axis=0, tiled=True)
    second = lax.all_gather(mine[:, half:], NARROW, axis=0, tiled=True)
    down = (jnp.dot(first, down_weight[:half], preferred_element_type=jnp.float32)
            + jnp.dot(second, down_weight[half:], preferred_element_type=jnp.float32)).astype(jnp.bfloat16)
    pieces = down.reshape(n_z, n_x, rows, down.shape[1])
    across = jnp.sum(lax.all_to_all(pieces, "x", 1, 1).astype(jnp.float32), axis=1).astype(jnp.bfloat16)
    return jnp.sum(lax.all_to_all(across, "z", 0, 0).astype(jnp.float32), axis=0).astype(jnp.bfloat16)


def solution(mesh):
    n_wide, n_narrow = mesh.devices.shape
    n_x = len({device.coords[0] for device in mesh.devices[:, 0]})
    view = Mesh(mesh.devices.reshape(n_wide // n_x, n_x, n_narrow // 2, 2), ("z", "x", "y", "core"))
    wide = ("z", "x")
    in_specs = (
        P(wide, NARROW),
        P(NARROW),
        P(wide, NARROW),
        P(wide, NARROW),
        P(wide, NARROW),
    )
    out_specs = P(wide, NARROW)
    return jax.shard_map(local, mesh=view, in_specs=in_specs, out_specs=out_specs, check_vma=False)
```

```python
import jax
import jax.numpy as jnp
from jax import lax
from jax.sharding import Mesh, PartitionSpec as P

EPS = 1e-05
NARROW = ("y", "core")


def local(tokens, norm_gain, gate_weight, up_weight, down_weight):
    width = gate_weight.shape[0]
    n_z = lax.axis_size("z")
    n_x = lax.axis_size("x")
    n_narrow = lax.axis_size(NARROW)
    model_width = tokens.shape[1] * n_narrow
    rows = tokens.shape[0]
    spread = jnp.broadcast_to(tokens[None], (n_z,) + tokens.shape)
    near = lax.all_to_all(spread, "z", 0, 0)
    spread = jnp.broadcast_to(near[:, None], (n_z, n_x) + tokens.shape)
    whole = lax.all_to_all(spread, "x", 1, 1).reshape(n_z * n_x * rows, tokens.shape[1])
    values = whole.astype(jnp.float32)
    partial = jnp.sum(values * values, axis=1)
    scaled = (values * norm_gain).astype(jnp.bfloat16)
    dims = (((1,), (1,)), ((), ()))
    joined = jnp.concatenate([gate_weight, up_weight], axis=0)
    pair = lax.dot_general(scaled, joined, dims, preferred_element_type=jnp.float32).astype(jnp.bfloat16)
    pair, partial = lax.optimization_barrier((pair, partial))
    part = lax.psum_scatter(pair, NARROW, scatter_dimension=0, tiled=True)
    squares = lax.psum(partial, NARROW)
    step = part.shape[0]
    start = lax.axis_index(NARROW) * step
    mine_sq = lax.dynamic_slice_in_dim(squares, start, step, 0)
    scale = lax.rsqrt(mine_sq / model_width + EPS)[:, None]
    sums = part.astype(jnp.float32)
    mine = (jax.nn.silu(sums[:, :width] * scale) * (sums[:, width:] * scale)).astype(jnp.bfloat16)
    half = width // 2
    first = lax.all_gather(mine[:, :half], NARROW, axis=0, tiled=True)
    second = lax.all_gather(mine[:, half:], NARROW, axis=0, tiled=True)
    down = (jnp.dot(first, down_weight[:half], preferred_element_type=jnp.float32)
            + jnp.dot(second, down_weight[half:], preferred_element_type=jnp.float32)).astype(jnp.bfloat16)
    pieces = down.reshape(n_z, n_x, rows, down.shape[1])
    across = jnp.sum(lax.all_to_all(pieces, "x", 1, 1).astype(jnp.float32), axis=1).astype(jnp.bfloat16)
    return jnp.sum(lax.all_to_all(across, "z", 0, 0).astype(jnp.float32), axis=0).astype(jnp.bfloat16)


def solution(mesh):
    n_wide, n_narrow = mesh.devices.shape
    n_x = len({device.coords[0] for device in mesh.devices[:, 0]})
    view = Mesh(mesh.devices.reshape(n_wide // n_x, n_x, n_narrow // 2, 2), ("z", "x", "y", "core"))
    wide = ("z", "x")
    in_specs = (
        P(wide, NARROW),
        P(NARROW),
        P(wide, NARROW),
        P(wide, NARROW),
        P(wide, NARROW),
    )
    out_specs = P(wide, NARROW)
    return jax.shard_map(local, mesh=view, in_specs=in_specs, out_specs=out_specs, check_vma=False)
```

```python
import jax
import jax.numpy as jnp
from jax import lax
from jax.sharding import Mesh, PartitionSpec as P

EPS = 1e-05
NARROW = ("y", "core")


def local(tokens, norm_gain, gate_weight, up_weight, down_weight):
    width = gate_weight.shape[0]
    n_z = lax.axis_size("z")
    n_x = lax.axis_size("x")
    n_narrow = lax.axis_size(NARROW)
    model_width = tokens.shape[1] * n_narrow
    rows = tokens.shape[0]
    spread = jnp.broadcast_to(tokens[None], (n_z,) + tokens.shape)
    near = lax.all_to_all(spread, "z", 0, 0)
    spread = jnp.broadcast_to(near[:, None], (n_z, n_x) + tokens.shape)
    whole = lax.all_to_all(spread, "x", 1, 1).reshape(n_z * n_x * rows, tokens.shape[1])
    values = whole.astype(jnp.float32)
    partial = jnp.sum(values * values, axis=1)
    scaled = (values * norm_gain).astype(jnp.bfloat16)
    dims = (((1,), (1,)), ((), ()))
    joined = jnp.concatenate([gate_weight, up_weight], axis=0)
    pair = lax.dot_general(scaled, joined, dims, preferred_element_type=jnp.float32).astype(jnp.bfloat16)
    n_y = lax.axis_size("y")
    n_c = lax.axis_size("core")
    step = pair.shape[0] // (n_y * n_c)
    pieces = pair.reshape(n_y, n_c, step, pair.shape[1])
    inner = jnp.sum(lax.all_to_all(pieces, "core", 1, 1).astype(jnp.float32), axis=1).astype(jnp.bfloat16)
    part = jnp.sum(lax.all_to_all(inner, "y", 0, 0).astype(jnp.float32), axis=0)
    shares = partial.reshape(n_y, n_c, step)
    shares = jnp.sum(lax.all_to_all(shares, "core", 1, 1), axis=1)
    mine_sq = jnp.sum(lax.all_to_all(shares, "y", 0, 0), axis=0)
    scale = lax.rsqrt(mine_sq / model_width + EPS)[:, None]
    sums = part.astype(jnp.float32)
    mine = (jax.nn.silu(sums[:, :width] * scale) * (sums[:, width:] * scale)).astype(jnp.bfloat16)
    half = width // 2
    first = lax.all_gather(mine[:, :half], NARROW, axis=0, tiled=True)
    second = lax.all_gather(mine[:, half:], NARROW, axis=0, tiled=True)
    down = (jnp.dot(first, down_weight[:half], preferred_element_type=jnp.float32)
            + jnp.dot(second, down_weight[half:], preferred_element_type=jnp.float32)).astype(jnp.bfloat16)
    pieces = down.reshape(n_z, n_x, rows, down.shape[1])
    across = jnp.sum(lax.all_to_all(pieces, "x", 1, 1).astype(jnp.float32), axis=1).astype(jnp.bfloat16)
    return jnp.sum(lax.all_to_all(across, "z", 0, 0).astype(jnp.float32), axis=0).astype(jnp.bfloat16)


def solution(mesh):
    n_wide, n_narrow = mesh.devices.shape
    n_x = len({device.coords[0] for device in mesh.devices[:, 0]})
    view = Mesh(mesh.devices.reshape(n_wide // n_x, n_x, n_narrow // 2, 2), ("z", "x", "y", "core"))
    wide = ("z", "x")
    in_specs = (
        P(wide, NARROW),
        P(NARROW),
        P(wide, NARROW),
        P(wide, NARROW),
        P(wide, NARROW),
    )
    out_specs = P(wide, NARROW)
    return jax.shard_map(local, mesh=view, in_specs=in_specs, out_specs=out_specs, check_vma=False)
```
